256 devices in a mesh: row: 64 (over z, x_hi, y), col: 4 (over x_lo, core).
Axes of the slice: x: 4 (x_hi: 2, x_lo: 2; x = x_hi * 2 + x_lo), y: 4, z: 8, core: 2. Of those that a mesh axis runs over, the one named last changes fastest.
Arguments:
- upper_tiles: bfloat16 [2048, 17, 4096], P(('row', 'col')), may hold values from -0.51 to 0.51, as said below
- block_columns: int32 [2048, 17], P(('row', 'col')), may hold values from -1 to 2047, as said below
Outputs:
- new_tiles: float32 [2048, 17, 4096], P(('row', 'col'))
- occupancy: float32 [], replicated
The draws below stay inside these ranges and needn't reach their ends.
Inputs may be any that keep to these rules, and one draw needn't show every extreme that they name: `block_columns`: slot 0 of block row i holds i. The following slots hold distinct block columns (i + s) mod 2048 with 1 <= s <= 16, in increasing s, and the remaining slots hold -1. Some block rows fill all 17 slots. `upper_tiles`: the block in slot 0 is symmetric.
All inputs are finite; a program needn't handle non-finite values.
Results may differ from the reference program's by a relative error of at most 0.0003.
Values may be sent and summed in bfloat16 or wider, within the bound.
No kernel may reach another device: no remote copies, remote signals or barrier semaphores. Data moves between devices by JAX's collectives and lax.ppermute only.
A program may use at most 128 MiB of HBM per device.

```python
import jax
import jax.numpy as jnp
import numpy as np
from jax import lax

BLOCK = 64
HALF = 16
ROWS_DEV = 8
NBLOCKS = 2048
SLOTS = 17
ORDER = 131072


def draw_block_columns(key, part):
    row_ids = jnp.arange(NBLOCKS, dtype=jnp.int32)
    threshold = 20 + 75 * row_ids // NBLOCKS
    chances = jax.random.randint(key, (NBLOCKS, HALF), 0, 100, dtype=jnp.int32)
    kept_mask = (chances < threshold[:, None]) | (row_ids % 7 == 0)[:, None]
    offsets = jnp.arange(1, HALF + 1, dtype=jnp.int32)[None, :]
    ranked = jnp.sort(jnp.where(kept_mask, offsets, offsets + HALF + 1), axis=1)
    listed = jnp.where(ranked <= HALF, (row_ids[:, None] + ranked) % NBLOCKS, -1)
    return jnp.concatenate([row_ids[:, None], listed], axis=1).astype(jnp.int32)


def draw_upper_tiles(key, part):
    tile_values = jax.random.truncated_normal(key, -6.0, 6.0, (NBLOCKS, SLOTS, BLOCK * BLOCK), jnp.float32) * 0.06
    diagonal = tile_values[:, 0].reshape(NBLOCKS, BLOCK, BLOCK)
    diagonal = (diagonal + jnp.swapaxes(diagonal, 1, 2)) * 0.7071
    tile_values = jnp.concatenate([diagonal.reshape(NBLOCKS, 1, BLOCK * BLOCK), tile_values[:, 1:]], axis=1)
    return tile_values.astype(jnp.bfloat16)


def setup_inputs(seed: int = 0) -> dict:
    arg_keys = jax.random.split(jax.random.key(seed), 3)
    upper_tiles = draw_upper_tiles(jax.random.fold_in(arg_keys[2], 71), 0)
    block_columns = draw_block_columns(jax.random.fold_in(arg_keys[2], 71), 0)
    return dict(upper_tiles=upper_tiles, block_columns=block_columns)


def entry_tables(rows_dev, half):
    band_width = half + 1
    window = rows_dev + 2 * half
    zero_index = window * band_width

    def lookup(row_pos, col_pos):
        if col_pos >= row_pos and col_pos - row_pos <= half:
            return row_pos * band_width + col_pos - row_pos, False
        if col_pos < row_pos and row_pos - col_pos <= half:
            return col_pos * band_width + row_pos - col_pos, True
        return zero_index, False

    left_index = np.zeros((rows_dev, window), np.int32)
    left_flip = np.zeros((rows_dev, window), np.bool_)
    for own_row in range(rows_dev):
        for other_row in range(window):
            left_index[own_row, other_row], left_flip[own_row, other_row] = lookup(half + own_row, other_row)
    right_index = np.zeros((window, rows_dev + half), np.int32)
    right_flip = np.zeros((window, rows_dev + half), np.bool_)
    for other_row in range(window):
        for column_pos in range(rows_dev + half):
            right_index[other_row, column_pos], right_flip[other_row, column_pos] = lookup(other_row, half + column_pos)
    return left_index, left_flip, right_index, right_flip


def flip_tiles(tiles, block):
    shaped = tiles.reshape(tiles.shape[:-1] + (block, block))
    return jnp.swapaxes(shaped, -1, -2).reshape(tiles.shape)


def reference(upper_tiles, block_columns):
    tile_size = BLOCK * BLOCK
    window_rows = ROWS_DEV + 2 * HALF
    span_cols = ROWS_DEV + HALF
    row_ids = jnp.arange(NBLOCKS, dtype=jnp.int32)
    slot_range = jnp.arange(SLOTS, dtype=jnp.int32)
    listed = block_columns >= 0
    offsets_of = jnp.mod(block_columns - row_ids[:, None], NBLOCKS).astype(jnp.int32)
    matches = listed[:, :, None] & (offsets_of[:, :, None] == slot_range[None, None, :])
    slot_of = jnp.sum(jnp.where(matches, slot_range[None, :, None], 0), axis=1).astype(jnp.int32)
    present = jnp.any(matches, axis=1)
    band = jax.vmap(lambda tiles, picks: tiles[picks])(upper_tiles, slot_of)
    band = jnp.where(present[:, :, None], band, jnp.zeros((), upper_tiles.dtype))
    padded = jnp.concatenate([band[NBLOCKS - HALF:], band, band[:HALF]], axis=0)
    left_np, left_flip_np, right_np, right_flip_np = entry_tables(ROWS_DEV, HALF)
    left_index = jnp.asarray(left_np)
    left_flip = jnp.asarray(left_flip_np)
    right_index = jnp.asarray(right_np)
    right_flip = jnp.asarray(right_flip_np)
    local_rows = jnp.arange(ROWS_DEV, dtype=jnp.int32)

    def one_group(group):
        start = (group * ROWS_DEV).astype(jnp.int32)
        window = lax.dynamic_slice_in_dim(padded, start, window_rows, 0)
        flat = jnp.concatenate([window.reshape(window_rows * SLOTS, tile_size), jnp.zeros((1, tile_size), window.dtype)], axis=0)
        left = flat[left_index]
        left = jnp.where(left_flip[:, :, None], flip_tiles(left, BLOCK), left)
        right = flat[right_index]
        right = jnp.where(right_flip[:, :, None], flip_tiles(right, BLOCK), right)
        left = left.astype(jnp.float32).reshape(ROWS_DEV, window_rows, BLOCK, BLOCK)
        right = right.astype(jnp.float32).reshape(window_rows, span_cols, BLOCK, BLOCK)
        product = jnp.einsum("rjab,jkbc->rkac", left, right, precision=lax.Precision.HIGHEST)
        product = product.reshape(ROWS_DEV, span_cols, tile_size)
        own_tiles = lax.dynamic_slice_in_dim(upper_tiles, start, ROWS_DEV, 0)
        own_columns = lax.dynamic_slice_in_dim(block_columns, start, ROWS_DEV, 0)
        own_ids = start + local_rows
        own_valid = own_columns >= 0
        own_offsets = jnp.mod(own_columns - own_ids[:, None], NBLOCKS).astype(jnp.int32)
        target = jnp.where(own_valid, own_offsets + local_rows[:, None], 0).astype(jnp.int32)
        picked = jax.vmap(lambda rows_of, picks: rows_of[picks])(product, target)
        fresh = jnp.where(own_valid[:, :, None], 2.0 * own_tiles.astype(jnp.float32) - picked, jnp.zeros((), jnp.float32))
        diag_product = product[local_rows, local_rows].reshape(ROWS_DEV, BLOCK, BLOCK)
        diag_own = own_tiles[:, 0].astype(jnp.float32).reshape(ROWS_DEV, BLOCK, BLOCK)
        trace_part = jnp.sum(2.0 * jnp.diagonal(diag_own, axis1=1, axis2=2) - jnp.diagonal(diag_product, axis1=1, axis2=2))
        return fresh, trace_part

    fresh_all, traces = lax.map(one_group, jnp.arange(NBLOCKS // ROWS_DEV, dtype=jnp.int32))
    new_tiles = fresh_all.reshape(NBLOCKS, SLOTS, tile_size)
    occupancy = (jnp.sum(traces) / ORDER).astype(jnp.float32)
    return new_tiles, occupancy
```

```python
import math

import jax
import jax.numpy as jnp
import numpy as np
from jax import lax
from jax.sharding import PartitionSpec as P


def from_behind(shard, axis, by):
    length = lax.axis_size(axis)
    return lax.ppermute(shard, axis, [(i, (i + by) % length) for i in range(length)])


def entry_tables(rows_dev, half):
    band_width = half + 1
    window = rows_dev + 2 * half
    zero_index = window * band_width
    flipped_base = zero_index + 1

    def lookup(row_pos, col_pos):
        if col_pos >= row_pos and col_pos - row_pos <= half:
            return row_pos * band_width + col_pos - row_pos
        if col_pos < row_pos and row_pos - col_pos <= half:
            return flipped_base + col_pos * band_width + row_pos - col_pos
        return zero_index

    left_index = np.zeros((rows_dev, window), np.int32)
    for own_row in range(rows_dev):
        for other_row in range(window):
            left_index[own_row, other_row] = lookup(half + own_row, other_row)
    right_index = np.zeros((window, rows_dev + half), np.int32)
    for other_row in range(window):
        for column_pos in range(rows_dev + half):
            right_index[other_row, column_pos] = lookup(other_row, half + column_pos)
    return (left_index, right_index)


def flip_tiles(tiles, block):
    shaped = tiles.reshape(tiles.shape[:-1] + (block, block))
    return jnp.swapaxes(shaped, -1, -2).reshape(tiles.shape)


def body(upper_tiles, block_columns):
    rows_dev, slots, tile_size = upper_tiles.shape
    half = slots - 1
    block = math.isqrt(tile_size)
    devices = lax.axis_size(("row", "col"))
    nblocks = rows_dev * devices
    span_cols = rows_dev + half
    window_rows = rows_dev + 2 * half
    first_row = lax.axis_index(("row", "col")) * rows_dev
    local_rows = jnp.arange(rows_dev, dtype=jnp.int32)
    row_ids = first_row + local_rows
    slot_range = jnp.arange(slots, dtype=jnp.int32)
    listed = block_columns >= 0
    offsets_of = jnp.mod(block_columns - row_ids[:, None], nblocks)
    pick_band = (listed[:, :, None] & (offsets_of[:, :, None] == slot_range[None, None, :])).astype(
        jnp.bfloat16
    )
    own_band = jnp.einsum(
        "rso,rst->rot", pick_band, upper_tiles, preferred_element_type=jnp.float32
    ).astype(jnp.bfloat16)
    diag_own = upper_tiles[:, 0].astype(jnp.float32).reshape(rows_dev, block, block)
    own_trace = 2.0 * jnp.sum(jnp.diagonal(diag_own, axis1=1, axis2=2))
    weight = jnp.where(listed, jnp.where(slot_range[None, :] == 0, 1.0, 2.0), 0.0)
    squares = jnp.sum(jnp.square(upper_tiles.astype(jnp.float32)), axis=2)
    part = own_trace - jnp.sum(weight * squares)
    spread = jnp.where(lax.broadcasted_iota(jnp.int32, (8, 128), 1) == 0, part / 8.0, 0.0)
    parts = lax.all_gather(spread, ("row", "col"), tiled=True)
    total = jnp.sum(parts)
    reach = -(-half // rows_dev)
    below = []
    above = []
    moving = own_band
    for distance in range(reach):
        moving = from_behind(moving, ("row", "col"), 1)
        below.insert(0, moving)
    moving = own_band
    for distance in range(reach):
        moving = from_behind(moving, ("row", "col"), -1)
        above.append(moving)
    stacked = jnp.concatenate(below + [own_band] + above, axis=0)
    left_np, right_np = entry_tables(rows_dev, half)
    plain = stacked.reshape(window_rows * slots, tile_size)
    blank = jnp.zeros((1, tile_size), jnp.bfloat16)
    flat = jnp.concatenate([plain, blank, flip_tiles(plain, block)], axis=0)
    left = flat[jnp.asarray(left_np)].reshape(rows_dev, window_rows, block, block)
    right = flat[jnp.asarray(right_np)].reshape(window_rows, span_cols, block, block)
    product = jnp.einsum("rjab,jkbc->rkac", left, right, preferred_element_type=jnp.float32)
    product = product.reshape(rows_dev, span_cols, tile_size)
    target = jnp.where(listed, offsets_of + local_rows[:, None], -1)
    pick_new = (target[:, :, None] == jnp.arange(span_cols, dtype=jnp.int32)[None, None, :]).astype(
        jnp.float32
    )
    picked = jnp.einsum(
        "rsk,rkt->rst",
        pick_new,
        product,
        precision=lax.Precision.HIGHEST,
        preferred_element_type=jnp.float32,
    )
    new_tiles = jnp.where(listed[:, :, None], 2.0 * upper_tiles.astype(jnp.float32) - picked, 0.0)
    occupancy = (total / (nblocks * block)).astype(jnp.float32)
    return (new_tiles, occupancy)


def solution(mesh):
    placed = (P(("row", "col"), None, None), P(("row", "col"), None))
    return jax.shard_map(
        body,
        mesh=mesh,
        in_specs=placed,
        out_specs=(P(("row", "col"), None, None), P()),
        check_vma=False,
    )
```

```python
import math

import jax
import jax.numpy as jnp
import numpy as np
from jax import lax
from jax.sharding import PartitionSpec as P

AXES = ("row", "col")


def shifted(shard, by):
    length = lax.axis_size(AXES)
    return lax.ppermute(shard, AXES, [(i, (i + by) % length) for i in range(length)])


def butterfly_sum(value):
    length = lax.axis_size(AXES)
    step = 1
    while step < length:
        other = lax.ppermute(value, AXES, [(i, i ^ step) for i in range(length)])
        value = value + other
        step *= 2
    return value


def pad_slots(piece, before, after):
    return jnp.pad(piece, ((0, 0), (before, after), (0, 0), (0, 0)))


def body(upper_tiles, block_columns):
    rows_dev, slots, tile_size = upper_tiles.shape
    half = slots - 1
    block = math.isqrt(tile_size)
    devices = lax.axis_size(AXES)
    nblocks = rows_dev * devices
    window_rows = rows_dev + 2 * half
    span_cols = rows_dev + half
    first_row = lax.axis_index(AXES) * rows_dev
    local_rows = jnp.arange(rows_dev, dtype=jnp.int32)
    row_ids = first_row + local_rows
    slot_range = jnp.arange(slots, dtype=jnp.int32)
    listed = block_columns >= 0
    offsets_of = jnp.mod(block_columns - row_ids[:, None], nblocks)

    diag_own = upper_tiles[:, 0].astype(jnp.float32).reshape(rows_dev, block, block)
    own_trace = 2.0 * jnp.sum(jnp.diagonal(diag_own, axis1=1, axis2=2))
    weight = jnp.where(listed, jnp.where(slot_range[None, :] == 0, 1.0, 2.0), 0.0)
    squares = jnp.sum(jnp.square(upper_tiles.astype(jnp.float32)), axis=2)
    total = butterfly_sum(own_trace - jnp.sum(weight * squares))
    occupancy = (total / (nblocks * block)).astype(jnp.float32)

    tiles4 = upper_tiles.reshape(rows_dev, slots, block, block)
    pick_band = (listed[:, :, None] & (offsets_of[:, :, None] == slot_range[None, None, :])).astype(
        jnp.bfloat16
    )
    band = jnp.einsum(
        "rso,rspq->ropq", pick_band, tiles4, preferred_element_type=jnp.float32
    ).astype(jnp.bfloat16)

    cut = half - rows_dev + 1
    from_prev2 = shifted(band[:, cut:], 2)
    from_prev1 = shifted(band[:, 1:], 1)
    from_next1 = shifted(band[:, : slots - 1], -1)
    from_next2 = shifted(band[:, : slots - cut], -2)
    window = jnp.concatenate(
        [
            pad_slots(from_prev2, cut, 0),
            pad_slots(from_prev1, 1, 0),
            band,
            pad_slots(from_next1, 0, 1),
            pad_slots(from_next2, 0, cut),
        ],
        axis=0,
    )

    w_idx = lax.broadcasted_iota(jnp.int32, (window_rows, slots, 1, 1), 0)
    s_idx = lax.broadcasted_iota(jnp.int32, (window_rows, slots, 1, 1), 1)
    kept = jnp.where(w_idx + s_idx < window_rows, window, jnp.zeros((), window.dtype))
    padded = jnp.pad(kept, ((0, 0), (0, window_rows + 1 - slots), (0, 0), (0, 0)))
    flat = padded.reshape(window_rows * (window_rows + 1), block, block)
    upper = flat[: window_rows * window_rows].reshape(window_rows, window_rows, block, block)

    lower = jnp.transpose(upper, (1, 0, 3, 2))
    a_idx = lax.broadcasted_iota(jnp.int32, (span_cols, window_rows, 1, 1), 0) + half
    b_idx = lax.broadcasted_iota(jnp.int32, (span_cols, window_rows, 1, 1), 1)
    strip = upper[half:] + jnp.where(b_idx < a_idx, lower[half:], jnp.zeros((), lower.dtype))

    product = jnp.einsum(
        "abpq,cbrq->apcr", strip[:rows_dev], strip, preferred_element_type=jnp.float32
    )

    target = jnp.where(listed, offsets_of + local_rows[:, None], -1)
    pick_new = (target[:, :, None] == jnp.arange(span_cols, dtype=jnp.int32)[None, None, :]).astype(
        jnp.float32
    )
    picked = jnp.einsum(
        "rsc,rpcq->rspq",
        pick_new,
        product,
        precision=lax.Precision.HIGHEST,
        preferred_element_type=jnp.float32,
    ).reshape(rows_dev, slots, tile_size)
    new_tiles = jnp.where(listed[:, :, None], 2.0 * upper_tiles.astype(jnp.float32) - picked, 0.0)
    return (new_tiles, occupancy)


def solution(mesh):
    placed = (P(AXES, None, None), P(AXES, None))
    return jax.shard_map(
        body,
        mesh=mesh,
        in_specs=placed,
        out_specs=(P(AXES, None, None), P()),
        check_vma=False,
    )
```

```python
import functools
import math

import jax
import jax.numpy as jnp
from jax import lax
from jax.experimental import pallas as pl
from jax.experimental.pallas import tpu as pltpu
from jax.sharding import PartitionSpec as P

AXES = ("row", "col")
SUB, LANE = 32, 128


def shifted(shard, by):
    length = lax.axis_size(AXES)
    return lax.ppermute(shard, AXES, [(i, (i + by) % length) for i in range(length)])


def strip_kernel(rows_dev, half, block, cut,
                 sel_ref, lst_ref, tiles_ref, own_ref, p2_ref, p1_ref, n1_ref, n2_ref,
                 out_ref, strip_ref, band_out_ref):
    slots = half + 1
    window_rows = rows_dev + 2 * half
    span_cols = rows_dev + half

    def tile(w, s):
        if w < rows_dev:
            return p2_ref[w, s - cut] if s >= cut else None
        if w < 2 * rows_dev:
            return p1_ref[w - rows_dev, s - 1] if s >= 1 else None
        if w < half + rows_dev:
            return own_ref[w - half, s]
        if w < half + 2 * rows_dev:
            return n1_ref[w - half - rows_dev, s] if s < slots - 1 else None
        return n2_ref[w - half - 2 * rows_dev, s] if s < slots - cut else None

    strip_ref[...] = jnp.zeros(strip_ref.shape, strip_ref.dtype)
    for w in range(window_rows):
        for s in range(slots):
            flat = tile(w, s)
            if flat is None:
                continue
            t = flat.reshape(block, block)
            if w >= half and w + s < window_rows:
                strip_ref[pl.ds((w - half) * block, block), pl.ds((w + s) * block, block)] = t
            a = w + s - half
            if s >= 1 and 0 <= a < span_cols:
                strip_ref[pl.ds(a * block, block), pl.ds(w * block, block)] = t.T

    lhs = strip_ref[pl.ds(0, rows_dev * block), :]
    width = 256
    per = width // block
    for ct in range(span_cols * block // width):
        rhs = strip_ref[pl.ds(ct * width, width), :]
        res = lax.dot_general(lhs, rhs, (((1,), (1,)), ((), ())), preferred_element_type=jnp.float32)
        for r in range(rows_dev):
            for cc in range(per):
                o = ct * per + cc - r
                if 0 <= o <= half:
                    piece = res[r * block:(r + 1) * block, cc * block:(cc + 1) * block]
                    band_out_ref[r * slots + o] = piece.reshape(SUB, LANE)

    for i in range(rows_dev * slots):
        r, s = divmod(i, slots)
        value = 2.0 * tiles_ref[r, s].astype(jnp.float32) - band_out_ref[sel_ref[i]]
        out_ref[r, s] = jnp.where(lst_ref[i] > 0, value, 0.0)


def body(upper_tiles, block_columns):
    rows_dev, slots, tile_size = upper_tiles.shape
    half = slots - 1
    block = math.isqrt(tile_size)
    devices = lax.axis_size(AXES)
    nblocks = rows_dev * devices
    window_rows = rows_dev + 2 * half
    span_cols = rows_dev + half
    cut = half - rows_dev + 1
    first_row = lax.axis_index(AXES) * rows_dev
    local_rows = jnp.arange(rows_dev, dtype=jnp.int32)
    row_ids = first_row + local_rows
    slot_range = jnp.arange(slots, dtype=jnp.int32)
    listed = block_columns >= 0
    offsets_of = jnp.mod(block_columns - row_ids[:, None], nblocks)

    diag_own = upper_tiles[:, 0].astype(jnp.float32).reshape(rows_dev, block, block)
    own_trace = 2.0 * jnp.sum(jnp.diagonal(diag_own, axis1=1, axis2=2))
    weight = jnp.where(listed, jnp.where(slot_range[None, :] == 0, 1.0, 2.0), 0.0)
    squares = jnp.sum(jnp.square(upper_tiles.astype(jnp.float32)), axis=2)
    total = lax.psum(lax.psum(own_trace - jnp.sum(weight * squares), "col"), "row")
    occupancy = (total / (nblocks * block)).astype(jnp.float32)

    tiles = upper_tiles.reshape(rows_dev, slots, SUB, LANE)
    pick_band = (listed[:, :, None] & (offsets_of[:, :, None] == slot_range[None, None, :])).astype(
        jnp.bfloat16
    )
    band = jnp.einsum(
        "rso,rsmn->romn", pick_band, tiles, preferred_element_type=jnp.float32
    ).astype(jnp.bfloat16)

    from_prev2 = shifted(band[:, cut:], 2)
    from_prev1 = shifted(band[:, 1:], 1)
    from_next1 = shifted(band[:, : slots - 1], -1)
    from_next2 = shifted(band[:, : slots - cut], -2)

    sel = jnp.where(listed, local_rows[:, None] * slots + offsets_of, 0).reshape(-1).astype(jnp.int32)
    lst = listed.reshape(-1).astype(jnp.int32)
    vmem = pl.BlockSpec(memory_space=pltpu.VMEM)
    smem = pl.BlockSpec(memory_space=pltpu.SMEM)
    flops = 2 * rows_dev * block * window_rows * block * span_cols * block
    new_tiles = pl.pallas_call(
        functools.partial(strip_kernel, rows_dev, half, block, cut),
        out_shape=jax.ShapeDtypeStruct((rows_dev, slots, SUB, LANE), jnp.float32),
        in_specs=[smem, smem] + [vmem] * 6,
        out_specs=vmem,
        scratch_shapes=[
            pltpu.VMEM((span_cols * block, window_rows * block), jnp.bfloat16),
            pltpu.VMEM((rows_dev * slots, SUB, LANE), jnp.float32),
        ],
        compiler_params=pltpu.CompilerParams(vmem_limit_bytes=48 * 1024 * 1024),
        cost_estimate=pl.CostEstimate(flops=flops, bytes_accessed=8 * 1024 * 1024, transcendentals=0),
    )(sel, lst, tiles, band, from_prev2, from_prev1, from_next1, from_next2)
    return (new_tiles.reshape(rows_dev, slots, tile_size), occupancy)


def solution(mesh):
    placed = (P(AXES, None, None), P(AXES, None))
    return jax.shard_map(
        body,
        mesh=mesh,
        in_specs=placed,
        out_specs=(P(AXES, None, None), P()),
        check_vma=False,
    )
```

```python
import functools
import math

import jax
import jax.numpy as jnp
from jax import lax
from jax.experimental import pallas as pl
from jax.experimental.pallas import tpu as pltpu
from jax.sharding import PartitionSpec as P

AXES = ("row", "col")
SUB, LANE = 32, 128


def shifted(shard, by):
    length = lax.axis_size(AXES)
    return lax.ppermute(shard, AXES, [(i, (i + by) % length) for i in range(length)])


def strip_kernel(rows_dev, half, block, sources,
                 sel_ref, lst_ref, tiles_ref, own_ref, p2_ref, p1_ref, n1_ref, n2_ref,
                 out_ref, strip_ref, band_out_ref):
    slots = half + 1
    window_rows = rows_dev + 2 * half
    span_cols = rows_dev + half
    refs = {"p2": p2_ref, "p1": p1_ref, "own": own_ref, "n1": n1_ref, "n2": n2_ref}

    strip_ref[...] = jnp.zeros(strip_ref.shape, strip_ref.dtype)
    for w in range(window_rows):
        name, first, count = sources[w // rows_dev]
        src = refs[name]
        r = w % rows_dev
        if w >= half:
            length = min(count, window_rows - w - first)
            strip_ref[pl.ds((w - half) * block, block), pl.ds((w + first) * block, length * block)] = (
                src[r, :, pl.ds(0, length * block)]
            )
        s_lo = max(1, first, half - w)
        s_hi = min(first + count - 1, window_rows - 1 - w)
        if s_hi >= s_lo:
            n = s_hi - s_lo + 1
            chunk = src[r, :, pl.ds((s_lo - first) * block, n * block)]
            strip_ref[pl.ds((w + s_lo - half) * block, n * block), pl.ds(w * block, block)] = chunk.T

    lhs = strip_ref[pl.ds(0, rows_dev * block), :]
    width = 256
    per = width // block
    for ct in range(span_cols * block // width):
        rhs = strip_ref[pl.ds(ct * width, width), :]
        res = lax.dot_general(lhs, rhs, (((1,), (1,)), ((), ())), preferred_element_type=jnp.float32)
        for r in range(rows_dev):
            for cc in range(per):
                o = ct * per + cc - r
                if 0 <= o <= half:
                    band_out_ref[r * slots + o] = res[r * block:(r + 1) * block, cc * block:(cc + 1) * block]

    for i in range(rows_dev * slots):
        r, s = divmod(i, slots)
        value = 2.0 * tiles_ref[r, s].astype(jnp.float32) - band_out_ref[sel_ref[i]]
        out_ref[r, s] = jnp.where(lst_ref[i] > 0, value, 0.0)


def body(upper_tiles, block_columns):
    rows_dev, slots, tile_size = upper_tiles.shape
    half = slots - 1
    block = math.isqrt(tile_size)
    devices = lax.axis_size(AXES)
    nblocks = rows_dev * devices
    window_rows = rows_dev + 2 * half
    span_cols = rows_dev + half
    cut = half - rows_dev + 1
    first_row = lax.axis_index(AXES) * rows_dev
    local_rows = jnp.arange(rows_dev, dtype=jnp.int32)
    row_ids = first_row + local_rows
    slot_range = jnp.arange(slots, dtype=jnp.int32)
    listed = block_columns >= 0
    offsets_of = jnp.mod(block_columns - row_ids[:, None], nblocks)

    diag_own = upper_tiles[:, 0].astype(jnp.float32).reshape(rows_dev, block, block)
    own_trace = 2.0 * jnp.sum(jnp.diagonal(diag_own, axis1=1, axis2=2))
    weight = jnp.where(listed, jnp.where(slot_range[None, :] == 0, 1.0, 2.0), 0.0)
    squares = jnp.sum(jnp.square(upper_tiles.astype(jnp.float32)), axis=2)
    total = lax.psum(lax.psum(own_trace - jnp.sum(weight * squares), "col"), "row")
    occupancy = (total / (nblocks * block)).astype(jnp.float32)

    tiles = upper_tiles.reshape(rows_dev, slots, block, block)
    pick_band = (listed[:, :, None] & (offsets_of[:, :, None] == slot_range[None, None, :])).astype(
        jnp.bfloat16
    )
    strips = jnp.einsum(
        "rso,rspq->rpoq", pick_band, tiles, preferred_element_type=jnp.float32
    ).astype(jnp.bfloat16).reshape(rows_dev, block, slots * block)
    strips = jnp.pad(strips, ((0, 0), (0, 0), (0, block)))
    occupancy, strips = lax.optimization_barrier((occupancy, strips))

    from_prev2 = shifted(strips[:, :, cut * block : slots * block], 2)
    from_prev1 = shifted(strips[:, :, block : slots * block], 1)
    from_next1 = shifted(strips[:, :, : (slots - 1) * block], -1)
    from_next2 = shifted(strips[:, :, : (slots - cut) * block], -2)
    sources = (("p2", cut, slots - cut), ("p1", 1, slots - 1), ("own", 0, slots),
               ("n1", 0, slots - 1), ("n2", 0, slots - cut))

    sel = jnp.where(listed, local_rows[:, None] * slots + offsets_of, 0).reshape(-1).astype(jnp.int32)
    lst = listed.reshape(-1).astype(jnp.int32)
    vmem = pl.BlockSpec(memory_space=pltpu.VMEM)
    smem = pl.BlockSpec(memory_space=pltpu.SMEM)
    flops = 2 * rows_dev * block * window_rows * block * span_cols * block
    new_tiles = pl.pallas_call(
        functools.partial(strip_kernel, rows_dev, half, block, sources),
        out_shape=jax.ShapeDtypeStruct((rows_dev, slots, block, block), jnp.float32),
        in_specs=[smem, smem] + [vmem] * 6,
        out_specs=vmem,
        scratch_shapes=[
            pltpu.VMEM((span_cols * block, window_rows * block), jnp.bfloat16),
            pltpu.VMEM((rows_dev * slots, block, block), jnp.float32),
        ],
        compiler_params=pltpu.CompilerParams(vmem_limit_bytes=48 * 1024 * 1024),
        cost_estimate=pl.CostEstimate(flops=flops, bytes_accessed=8 * 1024 * 1024, transcendentals=0),
    )(sel, lst, tiles, strips, from_prev2, from_prev1, from_next1, from_next2)
    return (new_tiles.reshape(rows_dev, slots, tile_size), occupancy)


def solution(mesh):
    placed = (P(AXES, None, None), P(AXES, None))
    return jax.shard_map(
        body,
        mesh=mesh,
        in_specs=placed,
        out_specs=(P(AXES, None, None), P()),
        check_vma=False,
    )
```

```python
import functools
import math

import jax
import jax.numpy as jnp
from jax import lax
from jax.experimental import pallas as pl
from jax.experimental.pallas import tpu as pltpu
from jax.sharding import PartitionSpec as P

AXES = ("row", "col")
SUB, LANE = 32, 128


def shifted(shard, by):
    length = lax.axis_size(AXES)
    return lax.ppermute(shard, AXES, [(i, (i + by) % length) for i in range(length)])


def butterfly_sum(value):
    length = lax.axis_size(AXES)
    me = lax.axis_index(AXES)
    stride = 1
    while stride < length:
        radix = min(4, length // stride)
        digit = (me // stride) % radix
        got = [value]
        for j in range(1, radix):
            pairs = []
            for i in range(length):
                d = (i // stride) % radix
                pairs.append((i, i + (((d + j) % radix) - d) * stride))
            got.append(lax.ppermute(value, AXES, pairs))
        stacked = jnp.stack(got)
        ordered = [stacked[(digit - k) % radix] for k in range(radix)]
        while len(ordered) > 1:
            ordered = [ordered[i] + ordered[i + 1] for i in range(0, len(ordered), 2)]
        value = ordered[0]
        stride *= radix
    return value


def strip_kernel(rows_dev, half, block, sources,
                 sel_ref, lst_ref, tiles_ref, own_ref, p2_ref, p1_ref, n1_ref, n2_ref,
                 out_ref, strip_ref, band_out_ref):
    slots = half + 1
    window_rows = rows_dev + 2 * half
    span_cols = rows_dev + half
    refs = {"p2": p2_ref, "p1": p1_ref, "own": own_ref, "n1": n1_ref, "n2": n2_ref}

    strip_ref[...] = jnp.zeros(strip_ref.shape, strip_ref.dtype)
    for w in range(window_rows):
        name, first, count = sources[w // rows_dev]
        src = refs[name]
        r = w % rows_dev
        if w >= half:
            length = min(count, window_rows - w - first)
            strip_ref[pl.ds((w - half) * block, block), pl.ds((w + first) * block, length * block)] = (
                src[r, :, pl.ds(0, length * block)]
            )
        s_lo = max(1, first, half - w)
        s_hi = min(first + count - 1, window_rows - 1 - w)
        if s_hi >= s_lo:
            n = s_hi - s_lo + 1
            chunk = src[r, :, pl.ds((s_lo - first) * block, n * block)]
            strip_ref[pl.ds((w + s_lo - half) * block, n * block), pl.ds(w * block, block)] = chunk.T

    lhs = strip_ref[pl.ds(0, rows_dev * block), :]
    width = 256
    per = width // block
    for ct in range(span_cols * block // width):
        rhs = strip_ref[pl.ds(ct * width, width), :]
        res = lax.dot_general(lhs, rhs, (((1,), (1,)), ((), ())), preferred_element_type=jnp.float32)
        for r in range(rows_dev):
            for cc in range(per):
                o = ct * per + cc - r
                if 0 <= o <= half:
                    band_out_ref[r * slots + o] = res[r * block:(r + 1) * block, cc * block:(cc + 1) * block]

    for i in range(rows_dev * slots):
        r, s = divmod(i, slots)
        value = 2.0 * tiles_ref[r, s].astype(jnp.float32) - band_out_ref[sel_ref[i]]
        out_ref[r, s] = jnp.where(lst_ref[i] > 0, value, 0.0)


def body(upper_tiles, block_columns):
    rows_dev, slots, tile_size = upper_tiles.shape
    half = slots - 1
    block = math.isqrt(tile_size)
    devices = lax.axis_size(AXES)
    nblocks = rows_dev * devices
    window_rows = rows_dev + 2 * half
    span_cols = rows_dev + half
    cut = half - rows_dev + 1
    first_row = lax.axis_index(AXES) * rows_dev
    local_rows = jnp.arange(rows_dev, dtype=jnp.int32)
    row_ids = first_row + local_rows
    slot_range = jnp.arange(slots, dtype=jnp.int32)
    listed = block_columns >= 0
    offsets_of = jnp.mod(block_columns - row_ids[:, None], nblocks)

    diag_own = upper_tiles[:, 0].astype(jnp.float32).reshape(rows_dev, block, block)
    own_trace = 2.0 * jnp.sum(jnp.diagonal(diag_own, axis1=1, axis2=2))
    weight = jnp.where(listed, jnp.where(slot_range[None, :] == 0, 1.0, 2.0), 0.0)
    squares = jnp.sum(jnp.square(upper_tiles.astype(jnp.float32)), axis=2)
    total = butterfly_sum(own_trace - jnp.sum(weight * squares))
    occupancy = (total / (nblocks * block)).astype(jnp.float32)

    tiles = upper_tiles.reshape(rows_dev, slots, block, block)
    pick_band = (listed[:, :, None] & (offsets_of[:, :, None] == slot_range[None, None, :])).astype(
        jnp.bfloat16
    )
    strips = jnp.einsum(
        "rso,rspq->rpoq", pick_band, tiles, preferred_element_type=jnp.float32
    ).astype(jnp.bfloat16).reshape(rows_dev, block, slots * block)
    strips = jnp.pad(strips, ((0, 0), (0, 0), (0, block)))
    occupancy, strips = lax.optimization_barrier((occupancy, strips))

    from_prev2 = shifted(strips[:, :, cut * block : slots * block], 2)
    from_prev1 = shifted(strips[:, :, block : slots * block], 1)
    from_next1 = shifted(strips[:, :, : (slots - 1) * block], -1)
    from_next2 = shifted(strips[:, :, : (slots - cut) * block], -2)
    sources = (("p2", cut, slots - cut), ("p1", 1, slots - 1), ("own", 0, slots),
               ("n1", 0, slots - 1), ("n2", 0, slots - cut))

    sel = jnp.where(listed, local_rows[:, None] * slots + offsets_of, 0).reshape(-1).astype(jnp.int32)
    lst = listed.reshape(-1).astype(jnp.int32)
    vmem = pl.BlockSpec(memory_space=pltpu.VMEM)
    smem = pl.BlockSpec(memory_space=pltpu.SMEM)
    flops = 2 * rows_dev * block * window_rows * block * span_cols * block
    new_tiles = pl.pallas_call(
        functools.partial(strip_kernel, rows_dev, half, block, sources),
        out_shape=jax.ShapeDtypeStruct((rows_dev, slots, block, block), jnp.float32),
        in_specs=[smem, smem] + [vmem] * 6,
        out_specs=vmem,
        scratch_shapes=[
            pltpu.VMEM((span_cols * block, window_rows * block), jnp.bfloat16),
            pltpu.VMEM((rows_dev * slots, block, block), jnp.float32),
        ],
        compiler_params=pltpu.CompilerParams(vmem_limit_bytes=48 * 1024 * 1024),
        cost_estimate=pl.CostEstimate(flops=flops, bytes_accessed=8 * 1024 * 1024, transcendentals=0),
    )(sel, lst, tiles, strips, from_prev2, from_prev1, from_next1, from_next2)
    return (new_tiles.reshape(rows_dev, slots, tile_size), occupancy)


def solution(mesh):
    placed = (P(AXES, None, None), P(AXES, None))
    return jax.shard_map(
        body,
        mesh=mesh,
        in_specs=placed,
        out_specs=(P(AXES, None, None), P()),
        check_vma=False,
    )
```

```python
import functools
import math

import jax
import jax.numpy as jnp
from jax import lax
from jax.experimental import pallas as pl
from jax.experimental.pallas import tpu as pltpu
from jax.sharding import PartitionSpec as P

AXES = ("row", "col")
SUB, LANE = 32, 128


def shifted(shard, by):
    length = lax.axis_size(AXES)
    return lax.ppermute(shard, AXES, [(i, (i + by) % length) for i in range(length)])


def butterfly_sum(value):
    length = lax.axis_size(AXES)
    stride = 1
    while stride < length:
        value = value + lax.ppermute(value, AXES, [(i, i ^ stride) for i in range(length)])
        stride *= 2
    return value


def strip_kernel(rows_dev, half, block, sources,
                 sel_ref, lst_ref, tiles_ref, own_ref, p2_ref, p1_ref, n1_ref, n2_ref,
                 out_ref, strip_ref, band_out_ref):
    slots = half + 1
    window_rows = rows_dev + 2 * half
    span_cols = rows_dev + half
    refs = {"p2": p2_ref, "p1": p1_ref, "own": own_ref, "n1": n1_ref, "n2": n2_ref}

    strip_ref[...] = jnp.zeros(strip_ref.shape, strip_ref.dtype)
    for w in range(window_rows):
        name, first, count = sources[w // rows_dev]
        src = refs[name]
        r = w % rows_dev
        if w >= half:
            length = min(count, window_rows - w - first)
            strip_ref[pl.ds((w - half) * block, block), pl.ds((w + first) * block, length * block)] = (
                src[r, :, pl.ds(0, length * block)]
            )
        s_lo = max(1, first, half - w)
        s_hi = min(first + count - 1, window_rows - 1 - w)
        if s_hi >= s_lo:
            n = s_hi - s_lo + 1
            chunk = src[r, :, pl.ds((s_lo - first) * block, n * block)]
            strip_ref[pl.ds((w + s_lo - half) * block, n * block), pl.ds(w * block, block)] = chunk.T

    lhs = strip_ref[pl.ds(0, rows_dev * block), :]
    width = 256
    per = width // block
    for ct in range(span_cols * block // width):
        rhs = strip_ref[pl.ds(ct * width, width), :]
        res = lax.dot_general(lhs, rhs, (((1,), (1,)), ((), ())), preferred_element_type=jnp.float32)
        for r in range(rows_dev):
            for cc in range(per):
                o = ct * per + cc - r
                if 0 <= o <= half:
                    band_out_ref[r * slots + o] = res[r * block:(r + 1) * block, cc * block:(cc + 1) * block]

    for i in range(rows_dev * slots):
        r, s = divmod(i, slots)
        value = 2.0 * tiles_ref[r, s].astype(jnp.float32) - band_out_ref[sel_ref[i]]
        out_ref[r, s] = jnp.where(lst_ref[i] > 0, value, 0.0)


def body(upper_tiles, block_columns):
    rows_dev, slots, tile_size = upper_tiles.shape
    half = slots - 1
    block = math.isqrt(tile_size)
    devices = lax.axis_size(AXES)
    nblocks = rows_dev * devices
    window_rows = rows_dev + 2 * half
    span_cols = rows_dev + half
    cut = half - rows_dev + 1
    first_row = lax.axis_index(AXES) * rows_dev
    local_rows = jnp.arange(rows_dev, dtype=jnp.int32)
    row_ids = first_row + local_rows
    slot_range = jnp.arange(slots, dtype=jnp.int32)
    listed = block_columns >= 0
    offsets_of = jnp.mod(block_columns - row_ids[:, None], nblocks)

    diag_own = upper_tiles[:, 0].astype(jnp.float32).reshape(rows_dev, block, block)
    own_trace = 2.0 * jnp.sum(jnp.diagonal(diag_own, axis1=1, axis2=2))
    weight = jnp.where(listed, jnp.where(slot_range[None, :] == 0, 1.0, 2.0), 0.0)
    squares = jnp.sum(jnp.square(upper_tiles.astype(jnp.float32)), axis=2)
    total = butterfly_sum(own_trace - jnp.sum(weight * squares))
    occupancy = (total / (nblocks * block)).astype(jnp.float32)

    tiles = upper_tiles.reshape(rows_dev, slots, block, block)
    pick_band = (listed[:, :, None] & (offsets_of[:, :, None] == slot_range[None, None, :])).astype(
        jnp.bfloat16
    )
    strips = jnp.einsum(
        "rso,rspq->rpoq", pick_band, tiles, preferred_element_type=jnp.float32
    ).astype(jnp.bfloat16).reshape(rows_dev, block, slots * block)
    strips = jnp.pad(strips, ((0, 0), (0, 0), (0, block)))
    occupancy, strips = lax.optimization_barrier((occupancy, strips))

    from_prev2 = shifted(strips[:, :, (cut - 1) * block :], 2)
    from_prev1 = shifted(strips, 1)
    from_next1 = shifted(strips[:, :, : (slots - 1) * block], -1)
    from_next2 = shifted(strips[:, :, : (slots - cut) * block], -2)
    sources = (("p2", cut - 1, slots - cut + 1), ("p1", 0, slots), ("own", 0, slots),
               ("n1", 0, slots - 1), ("n2", 0, slots - cut))

    sel = jnp.where(listed, local_rows[:, None] * slots + offsets_of, 0).reshape(-1).astype(jnp.int32)
    lst = listed.reshape(-1).astype(jnp.int32)
    vmem = pl.BlockSpec(memory_space=pltpu.VMEM)
    smem = pl.BlockSpec(memory_space=pltpu.SMEM)
    flops = 2 * rows_dev * block * window_rows * block * span_cols * block
    new_tiles = pl.pallas_call(
        functools.partial(strip_kernel, rows_dev, half, block, sources),
        out_shape=jax.ShapeDtypeStruct((rows_dev, slots, block, block), jnp.float32),
        in_specs=[smem, smem] + [vmem] * 6,
        out_specs=vmem,
        scratch_shapes=[
            pltpu.VMEM((span_cols * block, window_rows * block), jnp.bfloat16),
            pltpu.VMEM((rows_dev * slots, block, block), jnp.float32),
        ],
        compiler_params=pltpu.CompilerParams(vmem_limit_bytes=48 * 1024 * 1024),
        cost_estimate=pl.CostEstimate(flops=flops, bytes_accessed=8 * 1024 * 1024, transcendentals=0),
    )(sel, lst, tiles, strips, from_prev2, from_prev1, from_next1, from_next2)
    return (new_tiles.reshape(rows_dev, slots, tile_size), occupancy)


def solution(mesh):
    placed = (P(AXES, None, None), P(AXES, None))
    return jax.shard_map(
        body,
        mesh=mesh,
        in_specs=placed,
        out_specs=(P(AXES, None, None), P()),
        check_vma=False,
    )
```

```python
import functools
import math

import jax
import jax.numpy as jnp
from jax import lax
from jax.experimental import pallas as pl
from jax.experimental.pallas import tpu as pltpu
from jax.sharding import PartitionSpec as P

AXES = ("row", "col")
SUB, LANE = 32, 128


def shifted(shard, by):
    length = lax.axis_size(AXES)
    return lax.ppermute(shard, AXES, [(i, (i + by) % length) for i in range(length)])


def butterfly_sum(value):
    length = lax.axis_size(AXES)
    stride = 1
    while stride < length:
        value = value + lax.ppermute(value, AXES, [(i, i ^ stride) for i in range(length)])
        stride *= 2
    return value


def strip_kernel(rows_dev, half, block, sources,
                 sel_ref, lst_ref, tiles_ref, own_ref, p2_ref, p1_ref, n1_ref, n2_ref,
                 out_ref, strip_ref, band_out_ref):
    slots = half + 1
    window_rows = rows_dev + 2 * half
    span_cols = rows_dev + half
    refs = {"p2": p2_ref, "p1": p1_ref, "own": own_ref, "n1": n1_ref, "n2": n2_ref}

    strip_ref[...] = jnp.zeros(strip_ref.shape, strip_ref.dtype)
    for w in range(window_rows):
        name, first, count = sources[w // rows_dev]
        src = refs[name]
        r = w % rows_dev
        if w >= half:
            length = min(count, window_rows - w - first)
            strip_ref[pl.ds((w - half) * block, block), pl.ds((w + first) * block, length * block)] = (
                src[r, :, pl.ds(0, length * block)]
            )
        s_lo = max(1, first, half - w)
        s_hi = min(first + count - 1, window_rows - 1 - w)
        if s_hi >= s_lo:
            n = s_hi - s_lo + 1
            chunk = src[r, :, pl.ds((s_lo - first) * block, n * block)]
            strip_ref[pl.ds((w + s_lo - half) * block, n * block), pl.ds(w * block, block)] = chunk.T

    lhs = strip_ref[pl.ds(0, rows_dev * block), :]
    width = 256
    per = width // block
    for ct in range(span_cols * block // width):
        rhs = strip_ref[pl.ds(ct * width, width), :]
        res = lax.dot_general(lhs, rhs, (((1,), (1,)), ((), ())), preferred_element_type=jnp.float32)
        for r in range(rows_dev):
            for cc in range(per):
                o = ct * per + cc - r
                if 0 <= o <= half:
                    band_out_ref[r * slots + o] = res[r * block:(r + 1) * block, cc * block:(cc + 1) * block]

    for i in range(rows_dev * slots):
        r, s = divmod(i, slots)
        value = 2.0 * tiles_ref[r, s].astype(jnp.float32) - band_out_ref[sel_ref[i]]
        out_ref[r, s] = jnp.where(lst_ref[i] > 0, value, 0.0)


def body(upper_tiles, block_columns):
    rows_dev, slots, tile_size = upper_tiles.shape
    half = slots - 1
    block = math.isqrt(tile_size)
    devices = lax.axis_size(AXES)
    nblocks = rows_dev * devices
    window_rows = rows_dev + 2 * half
    span_cols = rows_dev + half
    cut = half - rows_dev + 1
    first_row = lax.axis_index(AXES) * rows_dev
    local_rows = jnp.arange(rows_dev, dtype=jnp.int32)
    row_ids = first_row + local_rows
    slot_range = jnp.arange(slots, dtype=jnp.int32)
    listed = block_columns >= 0
    offsets_of = jnp.mod(block_columns - row_ids[:, None], nblocks)

    diag_own = upper_tiles[:, 0].astype(jnp.float32).reshape(rows_dev, block, block)
    own_trace = 2.0 * jnp.sum(jnp.diagonal(diag_own, axis1=1, axis2=2))
    weight = jnp.where(listed, jnp.where(slot_range[None, :] == 0, 1.0, 2.0), 0.0)
    squares = jnp.sum(jnp.square(upper_tiles.astype(jnp.float32)), axis=2)
    total = butterfly_sum(own_trace - jnp.sum(weight * squares))
    occupancy = (total / (nblocks * block)).astype(jnp.float32)

    tiles = upper_tiles.reshape(rows_dev, slots, block, block)
    pick_band = (listed[:, :, None] & (offsets_of[:, :, None] == slot_range[None, None, :])).astype(
        jnp.bfloat16
    )
    strips = jnp.einsum(
        "rso,rspq->rpoq", pick_band, tiles, preferred_element_type=jnp.float32
    ).astype(jnp.bfloat16).reshape(rows_dev, block, slots * block)
    strips = jnp.pad(strips, ((0, 0), (0, 0), (0, block)))

    from_prev2 = shifted(strips[:, :, (cut - 1) * block :], 2)
    from_prev1 = shifted(strips, 1)
    from_next1 = shifted(strips[:, :, : (slots - 1) * block], -1)
    from_next2 = shifted(strips[:, :, : (slots - cut) * block], -2)
    sources = (("p2", cut - 1, slots - cut + 1), ("p1", 0, slots), ("own", 0, slots),
               ("n1", 0, slots - 1), ("n2", 0, slots - cut))

    sel = jnp.where(listed, local_rows[:, None] * slots + offsets_of, 0).reshape(-1).astype(jnp.int32)
    lst = listed.reshape(-1).astype(jnp.int32)
    vmem = pl.BlockSpec(memory_space=pltpu.VMEM)
    smem = pl.BlockSpec(memory_space=pltpu.SMEM)
    flops = 2 * rows_dev * block * window_rows * block * span_cols * block
    new_tiles = pl.pallas_call(
        functools.partial(strip_kernel, rows_dev, half, block, sources),
        out_shape=jax.ShapeDtypeStruct((rows_dev, slots, block, block), jnp.float32),
        in_specs=[smem, smem] + [vmem] * 6,
        out_specs=vmem,
        scratch_shapes=[
            pltpu.VMEM((span_cols * block, window_rows * block), jnp.bfloat16),
            pltpu.VMEM((rows_dev * slots, block, block), jnp.float32),
        ],
        compiler_params=pltpu.CompilerParams(vmem_limit_bytes=48 * 1024 * 1024),
        cost_estimate=pl.CostEstimate(flops=flops, bytes_accessed=8 * 1024 * 1024, transcendentals=0),
    )(sel, lst, tiles, strips, from_prev2, from_prev1, from_next1, from_next2)
    return (new_tiles.reshape(rows_dev, slots, tile_size), occupancy)


def solution(mesh):
    placed = (P(AXES, None, None), P(AXES, None))
    return jax.shard_map(
        body,
        mesh=mesh,
        in_specs=placed,
        out_specs=(P(AXES, None, None), P()),
        check_vma=False,
    )
```

```python
import functools
import math

import jax
import jax.numpy as jnp
from jax import lax
from jax.experimental import pallas as pl
from jax.experimental.pallas import tpu as pltpu
from jax.sharding import PartitionSpec as P

AXES = ("row", "col")
SUB, LANE = 32, 128


def shifted(shard, by):
    length = lax.axis_size(AXES)
    return lax.ppermute(shard, AXES, [(i, (i + by) % length) for i in range(length)])


def butterfly_sum(value):
    length = lax.axis_size(AXES)
    strides = [1 << k for k in range(length.bit_length() - 1)]
    order = strides[:1] + strides[5:] + strides[2:5] + strides[1:2] if length == 256 else strides
    for stride in order:
        value = value + lax.ppermute(value, AXES, [(i, i ^ stride) for i in range(length)])
    return value


def strip_kernel(rows_dev, half, block, sources,
                 sel_ref, lst_ref, tiles_ref, own_ref, p2_ref, p1_ref, n1_ref, n2_ref,
                 out_ref, strip_ref, band_out_ref):
    slots = half + 1
    window_rows = rows_dev + 2 * half
    span_cols = rows_dev + half
    refs = {"p2": p2_ref, "p1": p1_ref, "own": own_ref, "n1": n1_ref, "n2": n2_ref}

    strip_ref[...] = jnp.zeros(strip_ref.shape, strip_ref.dtype)
    for w in range(window_rows):
        name, first, count = sources[w // rows_dev]
        src = refs[name]
        r = w % rows_dev
        if w >= half:
            length = min(count, window_rows - w - first)
            strip_ref[pl.ds((w - half) * block, block), pl.ds((w + first) * block, length * block)] = (
                src[r, :, pl.ds(0, length * block)]
            )
        s_lo = max(1, first, half - w)
        s_hi = min(first + count - 1, window_rows - 1 - w)
        if s_hi >= s_lo:
            n = s_hi - s_lo + 1
            chunk = src[r, :, pl.ds((s_lo - first) * block, n * block)]
            strip_ref[pl.ds((w + s_lo - half) * block, n * block), pl.ds(w * block, block)] = chunk.T

    lhs = strip_ref[pl.ds(0, rows_dev * block), :]
    width = 256
    per = width // block
    for ct in range(span_cols * block // width):
        rhs = strip_ref[pl.ds(ct * width, width), :]
        res = lax.dot_general(lhs, rhs, (((1,), (1,)), ((), ())), preferred_element_type=jnp.float32)
        for r in range(rows_dev):
            for cc in range(per):
                o = ct * per + cc - r
                if 0 <= o <= half:
                    band_out_ref[r * slots + o] = res[r * block:(r + 1) * block, cc * block:(cc + 1) * block]

    for i in range(rows_dev * slots):
        r, s = divmod(i, slots)
        value = 2.0 * tiles_ref[r, s].astype(jnp.float32) - band_out_ref[sel_ref[i]]
        out_ref[r, s] = jnp.where(lst_ref[i] > 0, value, 0.0)


def body(upper_tiles, block_columns):
    rows_dev, slots, tile_size = upper_tiles.shape
    half = slots - 1
    block = math.isqrt(tile_size)
    devices = lax.axis_size(AXES)
    nblocks = rows_dev * devices
    window_rows = rows_dev + 2 * half
    span_cols = rows_dev + half
    cut = half - rows_dev + 1
    first_row = lax.axis_index(AXES) * rows_dev
    local_rows = jnp.arange(rows_dev, dtype=jnp.int32)
    row_ids = first_row + local_rows
    slot_range = jnp.arange(slots, dtype=jnp.int32)
    listed = block_columns >= 0
    offsets_of = jnp.mod(block_columns - row_ids[:, None], nblocks)

    diag_own = upper_tiles[:, 0].astype(jnp.float32).reshape(rows_dev, block, block)
    own_trace = 2.0 * jnp.sum(jnp.diagonal(diag_own, axis1=1, axis2=2))
    weight = jnp.where(listed, jnp.where(slot_range[None, :] == 0, 1.0, 2.0), 0.0)
    squares = jnp.sum(jnp.square(upper_tiles.astype(jnp.float32)), axis=2)
    total = butterfly_sum(own_trace - jnp.sum(weight * squares))
    occupancy = (total / (nblocks * block)).astype(jnp.float32)

    tiles = upper_tiles.reshape(rows_dev, slots, block, block)
    pick_band = (listed[:, :, None] & (offsets_of[:, :, None] == slot_range[None, None, :])).astype(
        jnp.bfloat16
    )
    strips = jnp.einsum(
        "rso,rspq->rpoq", pick_band, tiles, preferred_element_type=jnp.float32
    ).astype(jnp.bfloat16).reshape(rows_dev, block, slots * block)
    strips = jnp.pad(strips, ((0, 0), (0, 0), (0, block)))

    from_prev2 = shifted(strips[:, :, (cut - 1) * block :], 2)
    from_prev1 = shifted(strips, 1)
    from_next1 = shifted(strips[:, :, : (slots - 1) * block], -1)
    from_next2 = shifted(strips[:, :, : (slots - cut) * block], -2)
    sources = (("p2", cut - 1, slots - cut + 1), ("p1", 0, slots), ("own", 0, slots),
               ("n1", 0, slots - 1), ("n2", 0, slots - cut))

    sel = jnp.where(listed, local_rows[:, None] * slots + offsets_of, 0).reshape(-1).astype(jnp.int32)
    lst = listed.reshape(-1).astype(jnp.int32)
    vmem = pl.BlockSpec(memory_space=pltpu.VMEM)
    smem = pl.BlockSpec(memory_space=pltpu.SMEM)
    flops = 2 * rows_dev * block * window_rows * block * span_cols * block
    new_tiles = pl.pallas_call(
        functools.partial(strip_kernel, rows_dev, half, block, sources),
        out_shape=jax.ShapeDtypeStruct((rows_dev, slots, block, block), jnp.float32),
        in_specs=[smem, smem] + [vmem] * 6,
        out_specs=vmem,
        scratch_shapes=[
            pltpu.VMEM((span_cols * block, window_rows * block), jnp.bfloat16),
            pltpu.VMEM((rows_dev * slots, block, block), jnp.float32),
        ],
        compiler_params=pltpu.CompilerParams(vmem_limit_bytes=48 * 1024 * 1024),
        cost_estimate=pl.CostEstimate(flops=flops, bytes_accessed=8 * 1024 * 1024, transcendentals=0),
    )(sel, lst, tiles, strips, from_prev2, from_prev1, from_next1, from_next2)
    return (new_tiles.reshape(rows_dev, slots, tile_size), occupancy)


def solution(mesh):
    placed = (P(AXES, None, None), P(AXES, None))
    return jax.shard_map(
        body,
        mesh=mesh,
        in_specs=placed,
        out_specs=(P(AXES, None, None), P()),
        check_vma=False,
    )
```

```python
import functools
import math

import jax
import jax.numpy as jnp
from jax import lax
from jax.experimental import pallas as pl
from jax.experimental.pallas import tpu as pltpu
from jax.sharding import PartitionSpec as P

AXES = ("row", "col")
SUB, LANE = 32, 128


def shifted(shard, by):
    length = lax.axis_size(AXES)
    return lax.ppermute(shard, AXES, [(i, (i + by) % length) for i in range(length)])


def butterfly_sum(value):
    length = lax.axis_size(AXES)
    strides = [1 << k for k in range(length.bit_length() - 1)]
    order = strides[:1] + strides[5:] + strides[2:5] + strides[1:2] if length == 256 else strides
    for stride in order:
        value = value + lax.ppermute(value, AXES, [(i, i ^ stride) for i in range(length)])
    return value


def strip_kernel(rows_dev, half, block, sources,
                 sel_ref, lst_ref, own_ref, p2_ref, p1_ref, n1_ref, n2_ref,
                 out_ref, strip_ref, band_out_ref):
    slots = half + 1
    window_rows = rows_dev + 2 * half
    span_cols = rows_dev + half
    refs = {"p2": p2_ref, "p1": p1_ref, "own": own_ref, "n1": n1_ref, "n2": n2_ref}

    strip_ref[...] = jnp.zeros(strip_ref.shape, strip_ref.dtype)
    for w in range(window_rows):
        name, first, count = sources[w // rows_dev]
        src = refs[name]
        r = w % rows_dev
        if w >= half:
            length = min(count, window_rows - w - first)
            strip_ref[pl.ds((w - half) * block, block), pl.ds((w + first) * block, length * block)] = (
                src[r, :, pl.ds(0, length * block)]
            )
        s_lo = max(1, first, half - w)
        s_hi = min(first + count - 1, window_rows - 1 - w)
        if s_hi >= s_lo:
            n = s_hi - s_lo + 1
            chunk = src[r, :, pl.ds((s_lo - first) * block, n * block)]
            strip_ref[pl.ds((w + s_lo - half) * block, n * block), pl.ds(w * block, block)] = chunk.T

    lhs = strip_ref[pl.ds(0, rows_dev * block), :]
    width = 256
    per = width // block
    for ct in range(span_cols * block // width):
        rhs = strip_ref[pl.ds(ct * width, width), :]
        res = lax.dot_general(lhs, rhs, (((1,), (1,)), ((), ())), preferred_element_type=jnp.float32)
        for r in range(rows_dev):
            for cc in range(per):
                o = ct * per + cc - r
                if 0 <= o <= half:
                    band_out_ref[r * slots + o] = res[r * block:(r + 1) * block, cc * block:(cc + 1) * block]

    for i in range(rows_dev * slots):
        r, s = divmod(i, slots)
        out_ref[r, s] = jnp.where(lst_ref[i] > 0, band_out_ref[sel_ref[i]], 0.0)


def body(upper_tiles, block_columns):
    rows_dev, slots, tile_size = upper_tiles.shape
    half = slots - 1
    block = math.isqrt(tile_size)
    devices = lax.axis_size(AXES)
    nblocks = rows_dev * devices
    window_rows = rows_dev + 2 * half
    span_cols = rows_dev + half
    cut = half - rows_dev + 1
    first_row = lax.axis_index(AXES) * rows_dev
    local_rows = jnp.arange(rows_dev, dtype=jnp.int32)
    row_ids = first_row + local_rows
    slot_range = jnp.arange(slots, dtype=jnp.int32)
    listed = block_columns >= 0
    offsets_of = jnp.mod(block_columns - row_ids[:, None], nblocks)

    diag_own = upper_tiles[:, 0].astype(jnp.float32).reshape(rows_dev, block, block)
    own_trace = 2.0 * jnp.sum(jnp.diagonal(diag_own, axis1=1, axis2=2))
    weight = jnp.where(listed, jnp.where(slot_range[None, :] == 0, 1.0, 2.0), 0.0)
    squares = jnp.sum(jnp.square(upper_tiles.astype(jnp.float32)), axis=2)
    total = butterfly_sum(own_trace - jnp.sum(weight * squares))
    occupancy = (total / (nblocks * block)).astype(jnp.float32)

    tiles = upper_tiles.reshape(rows_dev, slots, block, block)
    band_range = jnp.arange(slots + 1, dtype=jnp.int32)
    pick_band = (listed[:, :, None] & (offsets_of[:, :, None] == band_range[None, None, :])).astype(
        jnp.bfloat16
    )
    strips = jnp.einsum(
        "rso,rspq->rpoq", pick_band, tiles, preferred_element_type=jnp.float32
    ).astype(jnp.bfloat16).reshape(rows_dev, block, (slots + 1) * block)

    from_prev2 = shifted(strips[:, :, (cut - 1) * block :], 2)
    from_prev1 = shifted(strips, 1)
    from_next1 = shifted(strips[:, :, : (slots - 1) * block], -1)
    from_next2 = shifted(strips[:, :, : (slots - cut) * block], -2)
    sources = (("p2", cut - 1, slots - cut + 1), ("p1", 0, slots), ("own", 0, slots),
               ("n1", 0, slots - 1), ("n2", 0, slots - cut))

    sel = jnp.where(listed, local_rows[:, None] * slots + offsets_of, 0).reshape(-1).astype(jnp.int32)
    lst = listed.reshape(-1).astype(jnp.int32)
    vmem = pl.BlockSpec(memory_space=pltpu.VMEM)
    smem = pl.BlockSpec(memory_space=pltpu.SMEM)
    flops = 2 * rows_dev * block * window_rows * block * span_cols * block
    new_tiles = pl.pallas_call(
        functools.partial(strip_kernel, rows_dev, half, block, sources),
        out_shape=jax.ShapeDtypeStruct((rows_dev, slots, block, block), jnp.float32),
        in_specs=[smem, smem] + [vmem] * 5,
        out_specs=vmem,
        scratch_shapes=[
            pltpu.VMEM((span_cols * block, window_rows * block), jnp.bfloat16),
            pltpu.VMEM((rows_dev * slots, block, block), jnp.float32),
        ],
        compiler_params=pltpu.CompilerParams(vmem_limit_bytes=48 * 1024 * 1024),
        cost_estimate=pl.CostEstimate(flops=flops, bytes_accessed=8 * 1024 * 1024, transcendentals=0),
    )(sel, lst, strips, from_prev2, from_prev1, from_next1, from_next2)
    picked = new_tiles.reshape(rows_dev, slots, tile_size)
    new_tiles = jnp.where(listed[:, :, None], 2.0 * upper_tiles.astype(jnp.float32) - picked, 0.0)
    return (new_tiles, occupancy)


def solution(mesh):
    placed = (P(AXES, None, None), P(AXES, None))
    return jax.shard_map(
        body,
        mesh=mesh,
        in_specs=placed,
        out_specs=(P(AXES, None, None), P()),
        check_vma=False,
    )
```

```python
import functools
import math

import jax
import jax.numpy as jnp
from jax import lax
from jax.experimental import pallas as pl
from jax.experimental.pallas import tpu as pltpu
from jax.sharding import PartitionSpec as P

AXES = ("row", "col")
SUB, LANE = 32, 128


def shifted(shard, by):
    length = lax.axis_size(AXES)
    return lax.ppermute(shard, AXES, [(i, (i + by) % length) for i in range(length)])


def butterfly_sum(value):
    length = lax.axis_size(AXES)
    strides = [1 << k for k in range(length.bit_length() - 1)]
    order = strides[:1] + strides[5:] + strides[2:5] + strides[1:2] if length == 256 else strides
    for stride in order:
        value = value + lax.ppermute(value, AXES, [(i, i ^ stride) for i in range(length)])
    return value


def strip_kernel(rows_dev, half, block, sources,
                 sel_ref, lst_ref, own_ref, p2_ref, p1_ref, n1_ref, n2_ref,
                 out_ref, strip_ref, band_out_ref):
    slots = half + 1
    window_rows = rows_dev + 2 * half
    span_cols = rows_dev + half
    refs = {"p2": p2_ref, "p1": p1_ref, "own": own_ref, "n1": n1_ref, "n2": n2_ref}

    strip_ref[...] = jnp.zeros(strip_ref.shape, strip_ref.dtype)
    for w in range(window_rows):
        name, first, count = sources[w // rows_dev]
        src = refs[name]
        r = w % rows_dev
        if w >= half:
            length = min(count, window_rows - w - first)
            strip_ref[pl.ds((w - half) * block, block), pl.ds((w + first) * block, length * block)] = (
                src[r, :, pl.ds(0, length * block)]
            )
        s_lo = max(1, first, half - w)
        s_hi = min(first + count - 1, window_rows - 1 - w)
        if s_hi >= s_lo:
            n = s_hi - s_lo + 1
            chunk = src[r, :, pl.ds((s_lo - first) * block, n * block)]
            strip_ref[pl.ds((w + s_lo - half) * block, n * block), pl.ds(w * block, block)] = chunk.T

    lhs = strip_ref[pl.ds(0, rows_dev * block), :]
    width = 256
    per = width // block
    for ct in range(span_cols * block // width):
        rhs = strip_ref[pl.ds(ct * width, width), :]
        res = lax.dot_general(lhs, rhs, (((1,), (1,)), ((), ())), preferred_element_type=jnp.float32)
        for r in range(rows_dev):
            for cc in range(per):
                o = ct * per + cc - r
                if 0 <= o <= half:
                    piece = res[r * block:(r + 1) * block, cc * block:(cc + 1) * block]
                    band_out_ref[r * slots + o] = piece.reshape(SUB, LANE)

    for i in range(rows_dev * slots):
        r, s = divmod(i, slots)
        out_ref[r, s] = jnp.where(lst_ref[i] > 0, band_out_ref[sel_ref[i]], 0.0)


def body(upper_tiles, block_columns):
    rows_dev, slots, tile_size = upper_tiles.shape
    half = slots - 1
    block = math.isqrt(tile_size)
    devices = lax.axis_size(AXES)
    nblocks = rows_dev * devices
    window_rows = rows_dev + 2 * half
    span_cols = rows_dev + half
    cut = half - rows_dev + 1
    first_row = lax.axis_index(AXES) * rows_dev
    local_rows = jnp.arange(rows_dev, dtype=jnp.int32)
    row_ids = first_row + local_rows
    slot_range = jnp.arange(slots, dtype=jnp.int32)
    listed = block_columns >= 0
    offsets_of = jnp.mod(block_columns - row_ids[:, None], nblocks)

    diag_own = upper_tiles[:, 0].astype(jnp.float32).reshape(rows_dev, block, block)
    own_trace = 2.0 * jnp.sum(jnp.diagonal(diag_own, axis1=1, axis2=2))
    weight = jnp.where(listed, jnp.where(slot_range[None, :] == 0, 1.0, 2.0), 0.0)
    squares = jnp.sum(jnp.square(upper_tiles.astype(jnp.float32)), axis=2)
    total = butterfly_sum(own_trace - jnp.sum(weight * squares))
    occupancy = (total / (nblocks * block)).astype(jnp.float32)

    tiles = upper_tiles.reshape(rows_dev, slots, block, block)
    band_range = jnp.arange(slots + 1, dtype=jnp.int32)
    pick_band = (listed[:, :, None] & (offsets_of[:, :, None] == band_range[None, None, :])).astype(
        jnp.bfloat16
    )
    strips = jnp.einsum(
        "rso,rspq->rpoq", pick_band, tiles, preferred_element_type=jnp.float32
    ).astype(jnp.bfloat16).reshape(rows_dev, block, (slots + 1) * block)

    from_prev2 = shifted(strips[:, :, (cut - 1) * block :], 2)
    from_prev1 = shifted(strips, 1)
    from_next1 = shifted(strips[:, :, : (slots - 1) * block], -1)
    from_next2 = shifted(strips[:, :, : (slots - cut) * block], -2)
    sources = (("p2", cut - 1, slots - cut + 1), ("p1", 0, slots), ("own", 0, slots),
               ("n1", 0, slots - 1), ("n2", 0, slots - cut))

    sel = jnp.where(listed, local_rows[:, None] * slots + offsets_of, 0).reshape(-1).astype(jnp.int32)
    lst = listed.reshape(-1).astype(jnp.int32)
    vmem = pl.BlockSpec(memory_space=pltpu.VMEM)
    smem = pl.BlockSpec(memory_space=pltpu.SMEM)
    flops = 2 * rows_dev * block * window_rows * block * span_cols * block
    new_tiles = pl.pallas_call(
        functools.partial(strip_kernel, rows_dev, half, block, sources),
        out_shape=jax.ShapeDtypeStruct((rows_dev, slots, SUB, LANE), jnp.float32),
        in_specs=[smem, smem] + [vmem] * 5,
        out_specs=vmem,
        scratch_shapes=[
            pltpu.VMEM((span_cols * block, window_rows * block), jnp.bfloat16),
            pltpu.VMEM((rows_dev * slots, SUB, LANE), jnp.float32),
        ],
        compiler_params=pltpu.CompilerParams(vmem_limit_bytes=48 * 1024 * 1024),
        cost_estimate=pl.CostEstimate(flops=flops, bytes_accessed=8 * 1024 * 1024, transcendentals=0),
    )(sel, lst, strips, from_prev2, from_prev1, from_next1, from_next2)
    picked = new_tiles.reshape(rows_dev, slots, tile_size)
    new_tiles = jnp.where(listed[:, :, None], 2.0 * upper_tiles.astype(jnp.float32) - picked, 0.0)
    return (new_tiles, occupancy)


def solution(mesh):
    placed = (P(AXES, None, None), P(AXES, None))
    return jax.shard_map(
        body,
        mesh=mesh,
        in_specs=placed,
        out_specs=(P(AXES, None, None), P()),
        check_vma=False,
    )
```

```python
import functools
import math

import jax
import jax.numpy as jnp
from jax import lax
from jax.experimental import pallas as pl
from jax.experimental.pallas import tpu as pltpu
from jax.sharding import PartitionSpec as P

AXES = ("row", "col")
SUB, LANE = 32, 128


def shifted(shard, by):
    length = lax.axis_size(AXES)
    return lax.ppermute(shard, AXES, [(i, (i + by) % length) for i in range(length)])


def butterfly_sum(value):
    length = lax.axis_size(AXES)
    strides = [1 << k for k in range(length.bit_length() - 1)]
    order = strides[:1] + strides[5:] + strides[2:5] + strides[1:2] if length == 256 else strides
    for stride in order:
        value = value + lax.ppermute(value, AXES, [(i, i ^ stride) for i in range(length)])
    return value


def strip_kernel(rows_dev, half, block, sources,
                 sel_ref, lst_ref, own_ref, p2_ref, p1_ref, n1_ref, n2_ref,
                 out_ref, strip_ref, band_out_ref):
    slots = half + 1
    window_rows = rows_dev + 2 * half
    span_cols = rows_dev + half
    refs = {"p2": p2_ref, "p1": p1_ref, "own": own_ref, "n1": n1_ref, "n2": n2_ref}

    strip_ref[...] = jnp.zeros(strip_ref.shape, strip_ref.dtype)
    for w in range(window_rows):
        name, first, count = sources[w // rows_dev]
        src = refs[name]
        r = w % rows_dev
        if w >= half:
            length = min(count, window_rows - w - first)
            strip_ref[pl.ds((w - half) * block, block), pl.ds((w + first) * block, length * block)] = (
                src[r, :, pl.ds(0, length * block)]
            )
        s_lo = max(1, first, half - w)
        s_hi = min(first + count - 1, window_rows - 1 - w)
        if s_hi >= s_lo:
            n = s_hi - s_lo + 1
            chunk = src[r, :, pl.ds((s_lo - first) * block, n * block)]
            strip_ref[pl.ds((w + s_lo - half) * block, n * block), pl.ds(w * block, block)] = chunk.T

    lhs = strip_ref[pl.ds(0, rows_dev * block), :]
    width = 256
    per = width // block
    for ct in range(span_cols * block // width):
        rhs = strip_ref[pl.ds(ct * width, width), :]
        res = lax.dot_general(lhs, rhs, (((1,), (1,)), ((), ())), preferred_element_type=jnp.float32)
        for r in range(rows_dev):
            for cc in range(per):
                o = ct * per + cc - r
                if 0 <= o <= half:
                    band_out_ref[r * slots + o] = res[r * block:(r + 1) * block, cc * block:(cc + 1) * block]

    for i in range(rows_dev * slots):
        r, s = divmod(i, slots)
        out_ref[r, s] = jnp.where(lst_ref[i] > 0, band_out_ref[sel_ref[i]], 0.0)


def body(upper_tiles, block_columns):
    rows_dev, slots, tile_size = upper_tiles.shape
    half = slots - 1
    block = math.isqrt(tile_size)
    devices = lax.axis_size(AXES)
    nblocks = rows_dev * devices
    window_rows = rows_dev + 2 * half
    span_cols = rows_dev + half
    cut = half - rows_dev + 1
    first_row = lax.axis_index(AXES) * rows_dev
    local_rows = jnp.arange(rows_dev, dtype=jnp.int32)
    row_ids = first_row + local_rows
    slot_range = jnp.arange(slots, dtype=jnp.int32)
    listed = block_columns >= 0
    offsets_of = jnp.mod(block_columns - row_ids[:, None], nblocks)

    values = upper_tiles.astype(jnp.float32)
    weight = jnp.where(listed, jnp.where(slot_range[None, :] == 0, 1.0, 2.0), 0.0)
    on_diag = (lax.broadcasted_iota(jnp.int32, (1, slots, tile_size), 2) % (block + 1) == 0) & (
        lax.broadcasted_iota(jnp.int32, (1, slots, tile_size), 1) == 0
    )
    terms = jnp.where(on_diag, 2.0 * values, 0.0) - weight[:, :, None] * jnp.square(values)
    total = butterfly_sum(jnp.sum(terms))

    tiles = upper_tiles.reshape(rows_dev, slots, block, block)
    band_range = jnp.arange(slots + 1, dtype=jnp.int32)
    pick_band = (listed[:, :, None] & (offsets_of[:, :, None] == band_range[None, None, :])).astype(
        jnp.bfloat16
    )
    strips = jnp.einsum(
        "rso,rspq->rpoq", pick_band, tiles, preferred_element_type=jnp.float32
    ).astype(jnp.bfloat16).reshape(rows_dev, block, (slots + 1) * block)

    from_prev2 = shifted(strips[:, :, (cut - 1) * block :], 2)
    from_prev1 = shifted(strips, 1)
    from_next1 = shifted(strips[:, :, : (slots - 1) * block], -1)
    from_next2 = shifted(strips[:, :, : (slots - cut) * block], -2)
    sources = (("p2", cut - 1, slots - cut + 1), ("p1", 0, slots), ("own", 0, slots),
               ("n1", 0, slots - 1), ("n2", 0, slots - cut))

    total, from_prev2, from_prev1, from_next1, from_next2 = lax.optimization_barrier(
        (total, from_prev2, from_prev1, from_next1, from_next2)
    )
    occupancy = (total / (nblocks * block)).astype(jnp.float32)

    sel = jnp.where(listed, local_rows[:, None] * slots + offsets_of, 0).reshape(-1).astype(jnp.int32)
    lst = listed.reshape(-1).astype(jnp.int32)
    vmem = pl.BlockSpec(memory_space=pltpu.VMEM)
    smem = pl.BlockSpec(memory_space=pltpu.SMEM)
    flops = 2 * rows_dev * block * window_rows * block * span_cols * block
    new_tiles = pl.pallas_call(
        functools.partial(strip_kernel, rows_dev, half, block, sources),
        out_shape=jax.ShapeDtypeStruct((rows_dev, slots, block, block), jnp.float32),
        in_specs=[smem, smem] + [vmem] * 5,
        out_specs=vmem,
        scratch_shapes=[
            pltpu.VMEM((span_cols * block, window_rows * block), jnp.bfloat16),
            pltpu.VMEM((rows_dev * slots, block, block), jnp.float32),
        ],
        compiler_params=pltpu.CompilerParams(vmem_limit_bytes=48 * 1024 * 1024),
        cost_estimate=pl.CostEstimate(flops=flops, bytes_accessed=8 * 1024 * 1024, transcendentals=0),
    )(sel, lst, strips, from_prev2, from_prev1, from_next1, from_next2)
    picked = new_tiles.reshape(rows_dev, slots, tile_size)
    new_tiles = jnp.where(listed[:, :, None], 2.0 * upper_tiles.astype(jnp.float32) - picked, 0.0)
    return (new_tiles, occupancy)


def solution(mesh):
    placed = (P(AXES, None, None), P(AXES, None))
    return jax.shard_map(
        body,
        mesh=mesh,
        in_specs=placed,
        out_specs=(P(AXES, None, None), P()),
        check_vma=False,
    )
```
